32 devices in a mesh: tok: 4 (over y, x), feat: 8 (over z, core).
Axes of the slice: x: 2, y: 2, z: 4, core: 2. Of those that a mesh axis runs over, the one named last changes fastest.
Arguments:
- acts: bfloat16 [512, 8192], P('tok', 'feat'), may hold values from -6 to 6
- grad_out: bfloat16 [512, 28672], P('tok', 'feat'), may hold values from -6 to 6
- weight: bfloat16 [8192, 28672], P('tok', 'feat'), may hold values from -0.03125 to 0.03125
- block_rows: int32 [1024], P('feat'), may hold values from 0 to 63
- block_cols: int32 [1024], P('feat'), may hold values from 0 to 27
- block_count: int32 [8], P('feat'), may hold values from 1 to 128, as said below
Outputs:
- grad_in: bfloat16 [512, 8192], P('feat', 'tok')
- block_grads: bfloat16 [1024, 128, 128], P('feat', 'tok')
The draws below stay inside these ranges and needn't reach their ends.
Inputs may be any that keep to these rules, and one draw needn't show every extreme that they name: `block_count`: each feat shard lists at most 128 blocks; one shard lists exactly 128; listed blocks of a shard may repeat.
All inputs are finite; a program needn't handle non-finite values.
Results may differ from the reference program's by a relative error of at most 0.001.
Values may be sent and summed in bfloat16 or wider, within the bound.
No kernel may reach another device: no remote copies, remote signals or barrier semaphores. Data moves between devices by JAX's collectives and lax.ppermute only.
A program may use at most 128 MiB of HBM per device.

```python
import jax
import jax.numpy as jnp
from jax import lax

D = 8192
FF = 28672
BLK = 128
SLOTS = 128
TOKENS = 512
CB_DEV = 28
N_FEAT = 8


def draw_block_count(key, part):
    first_key, second_key = jax.random.split(jax.random.fold_in(key, 17))
    counts = jax.random.randint(first_key, (N_FEAT,), 1, SLOTS + 1)
    full_shard = jax.random.randint(second_key, (), 0, N_FEAT)
    counts = jnp.where(jnp.arange(N_FEAT) == full_shard, SLOTS, counts)
    return counts.astype(jnp.int32)


def place_ends(drawn, key, smallest, high):
    longest = drawn.shape.index(max(drawn.shape))
    spots = []
    for shift in (0, 1):
        where = [jax.random.randint(jax.random.fold_in(key, axis), (), 0, length) for axis, length in enumerate(drawn.shape)]
        where[longest] = (where[longest] + shift) % drawn.shape[longest]
        spots.append(tuple(where))
    return drawn.at[spots[0]].set(smallest).at[spots[1]].set(high)


def block_levels(key, dims, shards, smallest, high):
    loudness = 1.0
    for position, blocks in shards:
        heights = jax.random.uniform(jax.random.fold_in(jax.random.fold_in(key, 6), position), (blocks,), jnp.float32, smallest / len(shards), high / len(shards))
        loudness = loudness * jnp.repeat(jnp.exp(heights), dims[position] // blocks).reshape((-1,) + (1,) * (len(dims) - 1 - position))
    return loudness


def bell_draw(rng, dims, spread, reach, shards=(), kind=jnp.bfloat16):
    values = jax.random.normal(rng, dims, jnp.float32) * spread
    if len(shards) > 0:
        values = block_levels(rng, dims, shards, -0.22, 0.18) * values
    return jnp.clip(values, min=-reach, max=reach).astype(kind)


def setup_inputs(seed: int = 0) -> dict:
    key_of = jax.random.split(jax.random.key(seed), 7)
    acts = bell_draw(key_of[0], (TOKENS, D), 1.0, 6.0, ((0, 4), (1, 8)))
    grad_out = bell_draw(key_of[1], (TOKENS, FF), 1.0, 6.0, ((0, 4), (1, 8)))
    weight = bell_draw(key_of[2], (D, FF), FF ** -0.5, 0.03125, ((0, 4), (1, 8)))
    block_rows = place_ends(jax.random.randint(key_of[3], (N_FEAT * SLOTS,), 0, D // BLK), jax.random.fold_in(key_of[3], 1), 0, (D // BLK) - 1).astype(jnp.int32)
    block_cols = place_ends(jax.random.randint(key_of[4], (N_FEAT * SLOTS,), 0, CB_DEV), jax.random.fold_in(key_of[4], 1), 0, CB_DEV - 1).astype(jnp.int32)
    block_count = draw_block_count(jax.random.fold_in(key_of[6], 71), 0)
    return {"acts": acts, "grad_out": grad_out, "weight": weight, "block_rows": block_rows, "block_cols": block_cols, "block_count": block_count}


def reference(acts, grad_out, weight, block_rows, block_cols, block_count):
    grad_in = jnp.dot(grad_out, weight.T, preferred_element_type=jnp.float32).astype(jnp.bfloat16)

    def one_block(slot_id):
        shard_id = slot_id // SLOTS
        row_id = block_rows[slot_id].astype(jnp.int32)
        col_id = (shard_id * CB_DEV + block_cols[slot_id]).astype(jnp.int32)
        act_panel = lax.dynamic_slice_in_dim(acts, row_id * BLK, BLK, 1)
        grad_panel = lax.dynamic_slice_in_dim(grad_out, col_id * BLK, BLK, 1)
        block_tile = jnp.dot(act_panel.T, grad_panel, preferred_element_type=jnp.float32)
        active = (slot_id - shard_id * SLOTS) < block_count[shard_id]
        return jnp.where(active, block_tile, jnp.float32(0.0)).astype(jnp.bfloat16)

    block_grads = lax.map(one_block, jnp.arange(N_FEAT * SLOTS, dtype=jnp.int32))
    return grad_in, block_grads
```

```python
import functools

import jax
import jax.numpy as jnp
from jax import lax
from jax.experimental import pallas as pl
from jax.experimental.pallas import tpu as pltpu
from jax.sharding import PartitionSpec as P

BLK = 128
SLOTS_PER_STEP = 8


def xor_exchange(x, axis_name, n):
    out = [x]
    for m in range(1, n):
        out.append(lax.ppermute(x, axis_name, perm=[(a, a ^ m) for a in range(n)]))
    return out


def place_rows(pieces, me, axis=0):
    rows = pieces[0].shape[axis]
    shape = list(pieces[0].shape)
    shape[axis] = rows * len(pieces)
    out = jnp.zeros(shape, pieces[0].dtype)
    for m, piece in enumerate(pieces):
        out = lax.dynamic_update_slice_in_dim(out, piece, (me ^ m) * rows, axis)
    return out


def block_kernel(rows_ref, cols_ref, cnt_ref, a_ref, g_ref, o_ref):
    step = pl.program_id(0)
    for u in range(SLOTS_PER_STEP):
        s = step * SLOTS_PER_STEP + u
        a = a_ref[rows_ref[s]]
        g = g_ref[:, pl.ds(pl.multiple_of(cols_ref[s] * BLK, BLK), BLK)]
        tile = jnp.dot(a, g, preferred_element_type=jnp.float32)
        tile = jnp.where(s < cnt_ref[0], tile, jnp.float32(0.0))
        o_ref[u] = tile.astype(o_ref.dtype)


def block_tiles(rows, cols, count, acts_t, gout):
    n_slots = rows.shape[0]
    sub, tokens = acts_t.shape[1], acts_t.shape[2]
    grid_spec = pltpu.PrefetchScalarGridSpec(
        num_scalar_prefetch=3,
        grid=(n_slots // SLOTS_PER_STEP,),
        in_specs=[
            pl.BlockSpec(acts_t.shape, lambda g, r, c, n: (0, 0, 0)),
            pl.BlockSpec(gout.shape, lambda g, r, c, n: (0, 0)),
        ],
        out_specs=pl.BlockSpec((SLOTS_PER_STEP, sub, BLK), lambda g, r, c, n: (g, 0, 0)),
    )
    return pl.pallas_call(
        block_kernel,
        grid_spec=grid_spec,
        out_shape=jax.ShapeDtypeStruct((n_slots, sub, BLK), jnp.bfloat16),
        cost_estimate=pl.CostEstimate(
            flops=2 * n_slots * sub * tokens * BLK,
            bytes_accessed=acts_t.size * 2 + gout.size * 2 + n_slots * sub * BLK * 2,
            transcendentals=0,
        ),
    )(rows, cols, count, acts_t, gout)


def per_device(n_tok, acts, grad_out, weight, block_rows, block_cols, block_count):
    me = lax.axis_index("tok")
    tok_dev, d_dev = acts.shape
    sub = BLK // n_tok

    acts_pieces = acts.reshape(tok_dev, d_dev // BLK, n_tok, sub)
    send = [
        lax.dynamic_index_in_dim(acts_pieces, me ^ m, axis=2, keepdims=False)
        for m in range(n_tok)
    ]
    got = [send[0]] + [
        lax.ppermute(send[m], "tok", perm=[(a, a ^ m) for a in range(n_tok)])
        for m in range(1, n_tok)
    ]
    acts_sub = place_rows(got, me)
    acts_sub_t = jnp.transpose(acts_sub, (1, 2, 0))
    acts_t = lax.all_gather(acts_sub_t, "feat", axis=0, tiled=True)

    gout = place_rows(xor_exchange(grad_out, "tok", n_tok), me)

    partial_sums = lax.dot_general(
        gout, weight, (((1,), (1,)), ((), ())), preferred_element_type=jnp.float32
    )
    grad_in = lax.psum_scatter(partial_sums, "feat", scatter_dimension=0, tiled=True).astype(
        jnp.bfloat16
    )
    block_grads = block_tiles(block_rows, block_cols, block_count, acts_t, gout)
    return (grad_in, block_grads)


def solution(mesh):
    n_tok = mesh.shape["tok"]
    assert n_tok & (n_tok - 1) == 0
    in_specs = (
        P("tok", "feat"),
        P("tok", "feat"),
        P("tok", "feat"),
        P("feat"),
        P("feat"),
        P("feat"),
    )
    out_specs = (P("feat", "tok"), P("feat", "tok", None))
    return jax.shard_map(
        functools.partial(per_device, n_tok),
        mesh=mesh,
        in_specs=in_specs,
        out_specs=out_specs,
        check_vma=False,
    )
```

```python
import functools

import jax
import jax.numpy as jnp
from jax import lax
from jax.experimental import pallas as pl
from jax.experimental.pallas import tpu as pltpu
from jax.sharding import PartitionSpec as P

BLK = 128
SLOTS_PER_STEP = 8
CHUNKS = 4


def xor_exchange(x, axis_name, n):
    out = [x]
    for m in range(1, n):
        out.append(lax.ppermute(x, axis_name, perm=[(a, a ^ m) for a in range(n)]))
    return out


def place_rows(pieces, me, axis=0):
    rows = pieces[0].shape[axis]
    shape = list(pieces[0].shape)
    shape[axis] = rows * len(pieces)
    out = jnp.zeros(shape, pieces[0].dtype)
    for m, piece in enumerate(pieces):
        out = lax.dynamic_update_slice_in_dim(out, piece, (me ^ m) * rows, axis)
    return out


def block_kernel(rows_ref, cols_ref, cnt_ref, a_ref, g_ref, o_ref):
    step = pl.program_id(0)
    for u in range(SLOTS_PER_STEP):
        s = step * SLOTS_PER_STEP + u
        a = a_ref[rows_ref[s]]
        g = g_ref[:, pl.ds(pl.multiple_of(cols_ref[s] * BLK, BLK), BLK)]
        tile = jnp.dot(a, g, preferred_element_type=jnp.float32)
        tile = jnp.where(s < cnt_ref[0], tile, jnp.float32(0.0))
        o_ref[u] = tile.astype(o_ref.dtype)


def block_tiles(rows, cols, count, acts_t, gout):
    n_slots = rows.shape[0]
    sub, tokens = acts_t.shape[1], acts_t.shape[2]
    grid_spec = pltpu.PrefetchScalarGridSpec(
        num_scalar_prefetch=3,
        grid=(n_slots // SLOTS_PER_STEP,),
        in_specs=[
            pl.BlockSpec(acts_t.shape, lambda g, r, c, n: (0, 0, 0)),
            pl.BlockSpec(gout.shape, lambda g, r, c, n: (0, 0)),
        ],
        out_specs=pl.BlockSpec((SLOTS_PER_STEP, sub, BLK), lambda g, r, c, n: (g, 0, 0)),
    )
    return pl.pallas_call(
        block_kernel,
        grid_spec=grid_spec,
        out_shape=jax.ShapeDtypeStruct((n_slots, sub, BLK), jnp.bfloat16),
        cost_estimate=pl.CostEstimate(
            flops=2 * n_slots * sub * tokens * BLK,
            bytes_accessed=acts_t.size * 2 + gout.size * 2 + n_slots * sub * BLK * 2,
            transcendentals=0,
        ),
    )(rows, cols, count, acts_t, gout)


def per_device(n_tok, n_feat, chunks, acts, grad_out, weight, block_rows, block_cols, block_count):
    me_tok = lax.axis_index("tok")
    me_feat = lax.axis_index("feat")
    tok_dev, d_dev = acts.shape
    f_dev = grad_out.shape[1]
    tokens = tok_dev * n_tok
    out_rows = tokens // n_feat
    own = tok_dev // out_rows
    piece = out_rows // chunks
    sub = BLK // n_tok

    def chunked(x):
        x = x.reshape((own, chunks, piece) + x.shape[1:])
        return jnp.swapaxes(x, 0, 1).reshape((chunks, own * piece) + x.shape[3:])

    acts_c = chunked(acts).reshape(chunks, own * piece, d_dev // BLK, n_tok, sub)
    got = []
    for m in range(n_tok):
        part = lax.dynamic_index_in_dim(acts_c, me_tok ^ m, axis=3, keepdims=False)
        if m:
            part = lax.ppermute(part, "tok", perm=[(a, a ^ m) for a in range(n_tok)])
        got.append(part)
    acts_sub = place_rows(got, me_tok, axis=1)
    acts_sub_t = jnp.transpose(acts_sub.reshape(tokens, d_dev // BLK, sub), (1, 2, 0))
    acts_t = place_rows(xor_exchange(acts_sub_t, "feat", n_feat), me_feat)

    gout_c = chunked(grad_out)
    outs = []
    gathered = []
    for c in range(chunks):
        g = place_rows(xor_exchange(gout_c[c], "tok", n_tok), me_tok)
        gathered.append(g)
        partial_sums = lax.dot_general(
            g, weight, (((1,), (1,)), ((), ())), preferred_element_type=jnp.float32
        )
        outs.append(lax.psum_scatter(partial_sums, "feat", scatter_dimension=0, tiled=True))
    grad_in = jnp.concatenate(outs, axis=0).astype(jnp.bfloat16)
    gout = jnp.concatenate(gathered, axis=0)
    block_grads = block_tiles(block_rows, block_cols, block_count, acts_t, gout)
    return (grad_in, block_grads)


def solution(mesh):
    n_tok = mesh.shape["tok"]
    n_feat = mesh.shape["feat"]
    assert n_tok & (n_tok - 1) == 0 and n_feat & (n_feat - 1) == 0
    in_specs = (
        P("tok", "feat"),
        P("tok", "feat"),
        P("tok", "feat"),
        P("feat"),
        P("feat"),
        P("feat"),
    )
    out_specs = (P("feat", "tok"), P("feat", "tok", None))
    return jax.shard_map(
        functools.partial(per_device, n_tok, n_feat, CHUNKS),
        mesh=mesh,
        in_specs=in_specs,
        out_specs=out_specs,
        check_vma=False,
    )
```

```python
import functools

import jax
import jax.numpy as jnp
from jax import lax
from jax.experimental import pallas as pl
from jax.experimental.pallas import tpu as pltpu
from jax.sharding import PartitionSpec as P

BLK = 128
SLOTS_PER_STEP = 8


def xor_exchange(x, axis_name, n):
    out = [x]
    for m in range(1, n):
        out.append(lax.ppermute(x, axis_name, perm=[(a, a ^ m) for a in range(n)]))
    return out


def place_rows(pieces, me, axis=0):
    rows = pieces[0].shape[axis]
    shape = list(pieces[0].shape)
    shape[axis] = rows * len(pieces)
    out = jnp.zeros(shape, pieces[0].dtype)
    for m, piece in enumerate(pieces):
        out = lax.dynamic_update_slice_in_dim(out, piece, (me ^ m) * rows, axis)
    return out


def block_kernel(rows_ref, cols_ref, cnt_ref, a_ref, g_ref, o_ref):
    step = pl.program_id(0)
    for u in range(SLOTS_PER_STEP):
        s = step * SLOTS_PER_STEP + u
        a = a_ref[rows_ref[s]]
        g = g_ref[:, pl.ds(pl.multiple_of(cols_ref[s] * BLK, BLK), BLK)]
        tile = jnp.dot(a, g, preferred_element_type=jnp.float32)
        tile = jnp.where(s < cnt_ref[0], tile, jnp.float32(0.0))
        o_ref[u] = tile.astype(o_ref.dtype)


def block_tiles(rows, cols, count, acts_t, gout):
    n_slots = rows.shape[0]
    sub, tokens = acts_t.shape[1], acts_t.shape[2]
    grid_spec = pltpu.PrefetchScalarGridSpec(
        num_scalar_prefetch=3,
        grid=(n_slots // SLOTS_PER_STEP,),
        in_specs=[
            pl.BlockSpec(acts_t.shape, lambda g, r, c, n: (0, 0, 0)),
            pl.BlockSpec(gout.shape, lambda g, r, c, n: (0, 0)),
        ],
        out_specs=pl.BlockSpec((SLOTS_PER_STEP, sub, BLK), lambda g, r, c, n: (g, 0, 0)),
    )
    return pl.pallas_call(
        block_kernel,
        grid_spec=grid_spec,
        out_shape=jax.ShapeDtypeStruct((n_slots, sub, BLK), jnp.bfloat16),
        cost_estimate=pl.CostEstimate(
            flops=2 * n_slots * sub * tokens * BLK,
            bytes_accessed=acts_t.size * 2 + gout.size * 2 + n_slots * sub * BLK * 2,
            transcendentals=0,
        ),
    )(rows, cols, count, acts_t, gout)


def per_device(n_tok, acts, grad_out, weight, block_rows, block_cols, block_count):
    me = lax.axis_index("tok")
    tok_dev, d_dev = acts.shape
    sub = BLK // n_tok

    acts_pieces = acts.reshape(tok_dev, d_dev // BLK, n_tok, sub)
    send = [
        lax.dynamic_index_in_dim(acts_pieces, me ^ m, axis=2, keepdims=False)
        for m in range(n_tok)
    ]
    got = [send[0]] + [
        lax.ppermute(send[m], "tok", perm=[(a, a ^ m) for a in range(n_tok)])
        for m in range(1, n_tok)
    ]
    got, grad_out = lax.optimization_barrier((got, grad_out))
    acts_sub = place_rows(got, me)
    acts_sub_t = jnp.transpose(acts_sub, (1, 2, 0))
    acts_t = lax.all_gather(acts_sub_t, "feat", axis=0, tiled=True)

    gout = place_rows(xor_exchange(grad_out, "tok", n_tok), me)

    partial_sums = lax.dot_general(
        gout, weight, (((1,), (1,)), ((), ())), preferred_element_type=jnp.float32
    )
    grad_in = lax.psum_scatter(partial_sums, "feat", scatter_dimension=0, tiled=True).astype(
        jnp.bfloat16
    )
    block_grads = block_tiles(block_rows, block_cols, block_count, acts_t, gout)
    return (grad_in, block_grads)


def solution(mesh):
    n_tok = mesh.shape["tok"]
    assert n_tok & (n_tok - 1) == 0
    in_specs = (
        P("tok", "feat"),
        P("tok", "feat"),
        P("tok", "feat"),
        P("feat"),
        P("feat"),
        P("feat"),
    )
    out_specs = (P("feat", "tok"), P("feat", "tok", None))
    return jax.shard_map(
        functools.partial(per_device, n_tok),
        mesh=mesh,
        in_specs=in_specs,
        out_specs=out_specs,
        check_vma=False,
    )
```

```python
import functools

import jax
import jax.numpy as jnp
from jax import lax
from jax.experimental import pallas as pl
from jax.experimental.pallas import tpu as pltpu
from jax.sharding import PartitionSpec as P

BLK = 128
SLOTS_PER_STEP = 8


def xor_exchange(x, axis_name, n):
    out = [x]
    for m in range(1, n):
        out.append(lax.ppermute(x, axis_name, perm=[(a, a ^ m) for a in range(n)]))
    return out


def place_rows(pieces, me, axis=0):
    rows = pieces[0].shape[axis]
    shape = list(pieces[0].shape)
    shape[axis] = rows * len(pieces)
    out = jnp.zeros(shape, pieces[0].dtype)
    for m, piece in enumerate(pieces):
        out = lax.dynamic_update_slice_in_dim(out, piece, (me ^ m) * rows, axis)
    return out


def block_kernel(rows_ref, cols_ref, cnt_ref, a_ref, g_ref, o_ref):
    step = pl.program_id(0)
    for u in range(SLOTS_PER_STEP):
        s = step * SLOTS_PER_STEP + u
        a = a_ref[rows_ref[s]]
        g = g_ref[:, pl.ds(pl.multiple_of(cols_ref[s] * BLK, BLK), BLK)]
        tile = jnp.dot(a, g, preferred_element_type=jnp.float32)
        tile = jnp.where(s < cnt_ref[0], tile, jnp.float32(0.0))
        o_ref[u] = tile.astype(o_ref.dtype)


def block_tiles(rows, cols, count, acts_t, gout):
    n_slots = rows.shape[0]
    sub, tokens = acts_t.shape[1], acts_t.shape[2]
    grid_spec = pltpu.PrefetchScalarGridSpec(
        num_scalar_prefetch=3,
        grid=(n_slots // SLOTS_PER_STEP,),
        in_specs=[
            pl.BlockSpec(acts_t.shape, lambda g, r, c, n: (0, 0, 0)),
            pl.BlockSpec(gout.shape, lambda g, r, c, n: (0, 0)),
        ],
        out_specs=pl.BlockSpec((SLOTS_PER_STEP, sub, BLK), lambda g, r, c, n: (g, 0, 0)),
    )
    return pl.pallas_call(
        block_kernel,
        grid_spec=grid_spec,
        out_shape=jax.ShapeDtypeStruct((n_slots, sub, BLK), jnp.bfloat16),
        cost_estimate=pl.CostEstimate(
            flops=2 * n_slots * sub * tokens * BLK,
            bytes_accessed=acts_t.size * 2 + gout.size * 2 + n_slots * sub * BLK * 2,
            transcendentals=0,
        ),
    )(rows, cols, count, acts_t, gout)


def per_device(n_tok, acts, grad_out, weight, block_rows, block_cols, block_count):
    me = lax.axis_index("tok")
    tok_dev = acts.shape[0]
    sub = BLK // n_tok

    full_acts = lax.all_gather(acts, "feat", axis=1, tiled=True)
    row_blocks = full_acts.shape[1] // BLK
    acts_pieces = jnp.transpose(full_acts.reshape(tok_dev, row_blocks, n_tok, sub), (2, 1, 3, 0))

    gout = place_rows(xor_exchange(grad_out, "tok", n_tok), me)
    partial_sums = lax.dot_general(
        gout, weight, (((1,), (1,)), ((), ())), preferred_element_type=jnp.float32
    )
    grad_in = lax.psum_scatter(partial_sums, "feat", scatter_dimension=0, tiled=True).astype(
        jnp.bfloat16
    )

    acts_pieces, gout = lax.optimization_barrier((acts_pieces, gout))
    got = []
    for m in range(n_tok):
        part = lax.dynamic_index_in_dim(acts_pieces, me ^ m, axis=0, keepdims=False)
        if m:
            part = lax.ppermute(part, "tok", perm=[(a, a ^ m) for a in range(n_tok)])
        got.append(part)
    acts_t = place_rows(got, me, axis=2)
    block_grads = block_tiles(block_rows, block_cols, block_count, acts_t, gout)
    return (grad_in, block_grads)


def solution(mesh):
    n_tok = mesh.shape["tok"]
    assert n_tok & (n_tok - 1) == 0
    in_specs = (
        P("tok", "feat"),
        P("tok", "feat"),
        P("tok", "feat"),
        P("feat"),
        P("feat"),
        P("feat"),
    )
    out_specs = (P("feat", "tok"), P("feat", "tok", None))
    return jax.shard_map(
        functools.partial(per_device, n_tok),
        mesh=mesh,
        in_specs=in_specs,
        out_specs=out_specs,
        check_vma=False,
    )
```

```python
import functools

import jax
import jax.numpy as jnp
from jax import lax
from jax.experimental import pallas as pl
from jax.experimental.pallas import tpu as pltpu
from jax.sharding import PartitionSpec as P

BLK = 128
SLOTS_PER_STEP = 8


def xor_exchange(x, axis_name, n):
    out = [x]
    for m in range(1, n):
        out.append(lax.ppermute(x, axis_name, perm=[(a, a ^ m) for a in range(n)]))
    return out


def place_rows(pieces, me, axis=0):
    rows = pieces[0].shape[axis]
    shape = list(pieces[0].shape)
    shape[axis] = rows * len(pieces)
    out = jnp.zeros(shape, pieces[0].dtype)
    for m, piece in enumerate(pieces):
        out = lax.dynamic_update_slice_in_dim(out, piece, (me ^ m) * rows, axis)
    return out


def block_kernel(rows_ref, cols_ref, cnt_ref, a_ref, g_ref, o_ref):
    step = pl.program_id(0)
    for u in range(SLOTS_PER_STEP):
        s = step * SLOTS_PER_STEP + u
        a = a_ref[rows_ref[s]]
        g = g_ref[:, pl.ds(pl.multiple_of(cols_ref[s] * BLK, BLK), BLK)]
        tile = jnp.dot(a, g, preferred_element_type=jnp.float32)
        tile = jnp.where(s < cnt_ref[0], tile, jnp.float32(0.0))
        o_ref[u] = tile.astype(o_ref.dtype)


def block_tiles(rows, cols, count, acts_t, gout):
    n_slots = rows.shape[0]
    sub, tokens = acts_t.shape[1], acts_t.shape[2]
    grid_spec = pltpu.PrefetchScalarGridSpec(
        num_scalar_prefetch=3,
        grid=(n_slots // SLOTS_PER_STEP,),
        in_specs=[
            pl.BlockSpec(acts_t.shape, lambda g, r, c, n: (0, 0, 0)),
            pl.BlockSpec(gout.shape, lambda g, r, c, n: (0, 0)),
        ],
        out_specs=pl.BlockSpec((SLOTS_PER_STEP, sub, BLK), lambda g, r, c, n: (g, 0, 0)),
    )
    return pl.pallas_call(
        block_kernel,
        grid_spec=grid_spec,
        out_shape=jax.ShapeDtypeStruct((n_slots, sub, BLK), jnp.bfloat16),
        cost_estimate=pl.CostEstimate(
            flops=2 * n_slots * sub * tokens * BLK,
            bytes_accessed=acts_t.size * 2 + gout.size * 2 + n_slots * sub * BLK * 2,
            transcendentals=0,
        ),
    )(rows, cols, count, acts_t, gout)


def feat_all_gather(x, n_feat, me_feat):
    core = me_feat % 2
    zs = [x] + [
        lax.ppermute(x, "feat", perm=[(a, a ^ m) for a in range(n_feat)])
        for m in range(2, n_feat, 2)
    ]
    mine = place_rows([piece[None] for piece in zs], me_feat // 2, axis=0)
    other = lax.ppermute(mine, "feat", perm=[(a, a ^ 1) for a in range(n_feat)])
    both = place_rows([mine[:, None], other[:, None]], core, axis=1)
    return jnp.transpose(both, (2, 0, 1, 3)).reshape(x.shape[0], -1)


def feat_reduce_scatter(h, n_feat, me_feat):
    core = me_feat % 2
    z = me_feat // 2
    h = h.reshape((n_feat // 2, 2, h.shape[0] // n_feat) + h.shape[1:])
    send = lax.dynamic_index_in_dim(h, 1 - core, axis=1, keepdims=False)
    keep = lax.dynamic_index_in_dim(h, core, axis=1, keepdims=False)
    chip = keep + lax.ppermute(send, "feat", perm=[(a, a ^ 1) for a in range(n_feat)])
    total = lax.dynamic_index_in_dim(chip, z, axis=0, keepdims=False)
    for m in range(1, n_feat // 2):
        part = lax.dynamic_index_in_dim(chip, z ^ m, axis=0, keepdims=False)
        total = total + lax.ppermute(part, "feat", perm=[(a, a ^ (2 * m)) for a in range(n_feat)])
    return total


def per_device(n_tok, n_feat, acts, grad_out, weight, block_rows, block_cols, block_count):
    me = lax.axis_index("tok")
    me_feat = lax.axis_index("feat")
    tok_dev = acts.shape[0]
    sub = BLK // n_tok

    full_acts = feat_all_gather(acts, n_feat, me_feat)
    row_blocks = full_acts.shape[1] // BLK
    acts_pieces = jnp.transpose(full_acts.reshape(tok_dev, row_blocks, n_tok, sub), (2, 1, 3, 0))

    gout = place_rows(xor_exchange(grad_out, "tok", n_tok), me)
    halves = []
    d_half = weight.shape[0] // 2
    for k in range(2):
        partial_sums = lax.dot_general(
            gout,
            weight[k * d_half : (k + 1) * d_half],
            (((1,), (1,)), ((), ())),
            preferred_element_type=jnp.float32,
        )
        halves.append(feat_reduce_scatter(partial_sums, n_feat, me_feat))
    grad_in = jnp.concatenate(halves, axis=1).astype(jnp.bfloat16)

    acts_pieces, gout = lax.optimization_barrier((acts_pieces, gout))
    got = []
    for m in range(n_tok):
        part = lax.dynamic_index_in_dim(acts_pieces, me ^ m, axis=0, keepdims=False)
        if m:
            part = lax.ppermute(part, "tok", perm=[(a, a ^ m) for a in range(n_tok)])
        got.append(part)
    acts_t = place_rows(got, me, axis=2)
    block_grads = block_tiles(block_rows, block_cols, block_count, acts_t, gout)
    return (grad_in, block_grads)


def solution(mesh):
    n_tok = mesh.shape["tok"]
    n_feat = mesh.shape["feat"]
    assert n_tok & (n_tok - 1) == 0 and n_feat & (n_feat - 1) == 0
    in_specs = (
        P("tok", "feat"),
        P("tok", "feat"),
        P("tok", "feat"),
        P("feat"),
        P("feat"),
        P("feat"),
    )
    out_specs = (P("feat", "tok"), P("feat", "tok", None))
    return jax.shard_map(
        functools.partial(per_device, n_tok, n_feat),
        mesh=mesh,
        in_specs=in_specs,
        out_specs=out_specs,
        check_vma=False,
    )
```

```python
import functools

import jax
import jax.numpy as jnp
from jax import lax
from jax.experimental import pallas as pl
from jax.experimental.pallas import tpu as pltpu
from jax.sharding import PartitionSpec as P

BLK = 128
SLOTS_PER_STEP = 8


def xor_exchange(x, axis_name, n):
    out = [x]
    for m in range(1, n):
        out.append(lax.ppermute(x, axis_name, perm=[(a, a ^ m) for a in range(n)]))
    return out


def place_rows(pieces, me, axis=0):
    rows = pieces[0].shape[axis]
    shape = list(pieces[0].shape)
    shape[axis] = rows * len(pieces)
    out = jnp.zeros(shape, pieces[0].dtype)
    for m, piece in enumerate(pieces):
        out = lax.dynamic_update_slice_in_dim(out, piece, (me ^ m) * rows, axis)
    return out


def block_kernel(rows_ref, cols_ref, cnt_ref, a_ref, g_ref, o_ref):
    step = pl.program_id(0)
    for u in range(SLOTS_PER_STEP):
        s = step * SLOTS_PER_STEP + u
        a = a_ref[rows_ref[s]]
        g = g_ref[:, pl.ds(pl.multiple_of(cols_ref[s] * BLK, BLK), BLK)]
        tile = jnp.dot(a, g, preferred_element_type=jnp.float32)
        tile = jnp.where(s < cnt_ref[0], tile, jnp.float32(0.0))
        o_ref[u] = tile.astype(o_ref.dtype)


def block_tiles(rows, cols, count, acts_t, gout):
    n_slots = rows.shape[0]
    sub, tokens = acts_t.shape[1], acts_t.shape[2]
    grid_spec = pltpu.PrefetchScalarGridSpec(
        num_scalar_prefetch=3,
        grid=(n_slots // SLOTS_PER_STEP,),
        in_specs=[
            pl.BlockSpec(acts_t.shape, lambda g, r, c, n: (0, 0, 0)),
            pl.BlockSpec(gout.shape, lambda g, r, c, n: (0, 0)),
        ],
        out_specs=pl.BlockSpec((SLOTS_PER_STEP, sub, BLK), lambda g, r, c, n: (g, 0, 0)),
    )
    return pl.pallas_call(
        block_kernel,
        grid_spec=grid_spec,
        out_shape=jax.ShapeDtypeStruct((n_slots, sub, BLK), jnp.bfloat16),
        cost_estimate=pl.CostEstimate(
            flops=2 * n_slots * sub * tokens * BLK,
            bytes_accessed=acts_t.size * 2 + gout.size * 2 + n_slots * sub * BLK * 2,
            transcendentals=0,
        ),
    )(rows, cols, count, acts_t, gout)


def feat_all_gather(x, n_feat, me_feat):
    core = me_feat % 2
    zs = [x] + [
        lax.ppermute(x, "feat", perm=[(a, a ^ m) for a in range(n_feat)])
        for m in range(2, n_feat, 2)
    ]
    mine = place_rows([piece[None] for piece in zs], me_feat // 2, axis=0)
    other = lax.ppermute(mine, "feat", perm=[(a, a ^ 1) for a in range(n_feat)])
    both = place_rows([mine[:, None], other[:, None]], core, axis=1)
    return jnp.transpose(both, (2, 0, 1, 3)).reshape(x.shape[0], -1)


def feat_reduce_scatter(h, n_feat, me_feat):
    core = me_feat % 2
    z = me_feat // 2
    h = h.reshape((n_feat // 2, 2, h.shape[0] // n_feat) + h.shape[1:])
    send = lax.dynamic_index_in_dim(h, 1 - core, axis=1, keepdims=False)
    keep = lax.dynamic_index_in_dim(h, core, axis=1, keepdims=False)
    chip = keep + lax.ppermute(send, "feat", perm=[(a, a ^ 1) for a in range(n_feat)])
    total = lax.dynamic_index_in_dim(chip, z, axis=0, keepdims=False)
    for m in range(1, n_feat // 2):
        part = lax.dynamic_index_in_dim(chip, z ^ m, axis=0, keepdims=False)
        total = total + lax.ppermute(part, "feat", perm=[(a, a ^ (2 * m)) for a in range(n_feat)])
    return total


def per_device(n_tok, n_feat, acts, grad_out, weight, block_rows, block_cols, block_count):
    me = lax.axis_index("tok")
    me_feat = lax.axis_index("feat")
    tok_dev = acts.shape[0]
    sub = BLK // n_tok

    full_acts = feat_all_gather(acts, n_feat, me_feat)
    row_blocks = full_acts.shape[1] // BLK
    acts_pieces = jnp.transpose(full_acts.reshape(tok_dev, row_blocks, n_tok, sub), (2, 1, 3, 0))

    gout = place_rows(xor_exchange(grad_out, "tok", n_tok), me)
    halves = []
    d_half = weight.shape[0] // 2
    for k in range(2):
        partial_sums = lax.dot_general(
            gout,
            weight[k * d_half : (k + 1) * d_half],
            (((1,), (1,)), ((), ())),
            preferred_element_type=jnp.float32,
        )
        halves.append(feat_reduce_scatter(partial_sums, n_feat, me_feat))

    acts_pieces, gout, halves[0] = lax.optimization_barrier((acts_pieces, gout, halves[0]))
    grad_in = jnp.concatenate(halves, axis=1).astype(jnp.bfloat16)
    got = []
    for m in range(n_tok):
        part = lax.dynamic_index_in_dim(acts_pieces, me ^ m, axis=0, keepdims=False)
        if m:
            part = lax.ppermute(part, "tok", perm=[(a, a ^ m) for a in range(n_tok)])
        got.append(part)
    acts_t = place_rows(got, me, axis=2)
    block_grads = block_tiles(block_rows, block_cols, block_count, acts_t, gout)
    return (grad_in, block_grads)


def solution(mesh):
    n_tok = mesh.shape["tok"]
    n_feat = mesh.shape["feat"]
    assert n_tok & (n_tok - 1) == 0 and n_feat & (n_feat - 1) == 0
    in_specs = (
        P("tok", "feat"),
        P("tok", "feat"),
        P("tok", "feat"),
        P("feat"),
        P("feat"),
        P("feat"),
    )
    out_specs = (P("feat", "tok"), P("feat", "tok", None))
    return jax.shard_map(
        functools.partial(per_device, n_tok, n_feat),
        mesh=mesh,
        in_specs=in_specs,
        out_specs=out_specs,
        check_vma=False,
    )
```

```python
import functools

import jax
import jax.numpy as jnp
from jax import lax
from jax.experimental import pallas as pl
from jax.experimental.pallas import tpu as pltpu
from jax.sharding import PartitionSpec as P

BLK = 128
SLOTS_PER_STEP = 8
F_CHUNKS = 2


def xor_exchange(x, axis_name, n):
    out = [x]
    for m in range(1, n):
        out.append(lax.ppermute(x, axis_name, perm=[(a, a ^ m) for a in range(n)]))
    return out


def place_rows(pieces, me, axis=0):
    rows = pieces[0].shape[axis]
    shape = list(pieces[0].shape)
    shape[axis] = rows * len(pieces)
    out = jnp.zeros(shape, pieces[0].dtype)
    for m, piece in enumerate(pieces):
        out = lax.dynamic_update_slice_in_dim(out, piece, (me ^ m) * rows, axis)
    return out


def block_kernel(rows_ref, cols_ref, cnt_ref, a_ref, g_ref, o_ref):
    step = pl.program_id(0)
    for u in range(SLOTS_PER_STEP):
        s = step * SLOTS_PER_STEP + u
        a = a_ref[rows_ref[s]]
        g = g_ref[:, pl.ds(pl.multiple_of(cols_ref[s] * BLK, BLK), BLK)]
        tile = jnp.dot(a, g, preferred_element_type=jnp.float32)
        tile = jnp.where(s < cnt_ref[0], tile, jnp.float32(0.0))
        o_ref[u] = tile.astype(o_ref.dtype)


def block_tiles(rows, cols, count, acts_t, gout):
    n_slots = rows.shape[0]
    sub, tokens = acts_t.shape[1], acts_t.shape[2]
    grid_spec = pltpu.PrefetchScalarGridSpec(
        num_scalar_prefetch=3,
        grid=(n_slots // SLOTS_PER_STEP,),
        in_specs=[
            pl.BlockSpec(acts_t.shape, lambda g, r, c, n: (0, 0, 0)),
            pl.BlockSpec(gout.shape, lambda g, r, c, n: (0, 0)),
        ],
        out_specs=pl.BlockSpec((SLOTS_PER_STEP, sub, BLK), lambda g, r, c, n: (g, 0, 0)),
    )
    return pl.pallas_call(
        block_kernel,
        grid_spec=grid_spec,
        out_shape=jax.ShapeDtypeStruct((n_slots, sub, BLK), jnp.bfloat16),
        cost_estimate=pl.CostEstimate(
            flops=2 * n_slots * sub * tokens * BLK,
            bytes_accessed=acts_t.size * 2 + gout.size * 2 + n_slots * sub * BLK * 2,
            transcendentals=0,
        ),
    )(rows, cols, count, acts_t, gout)


def matmul_kernel(*refs):
    if len(refs) == 4:
        g_ref, w_ref, acc_ref, o_ref = refs
    else:
        (g_ref, w_ref, o_ref), acc_ref = refs, None
    out = lax.dot_general(
        g_ref[...], w_ref[...], (((1,), (1,)), ((), ())), preferred_element_type=jnp.float32
    )
    if acc_ref is not None:
        out = out + acc_ref[...]
    o_ref[...] = out


def matmul_nt(g, w, acc):
    rows, depth = g.shape
    cols = w.shape[0]
    tile = min(cols, 512)
    in_specs = [
        pl.BlockSpec((rows, depth), lambda j: (0, 0)),
        pl.BlockSpec((tile, depth), lambda j: (j, 0)),
    ]
    args = [g, w]
    if acc is not None:
        in_specs.append(pl.BlockSpec((rows, tile), lambda j: (0, j)))
        args.append(acc)
    return pl.pallas_call(
        matmul_kernel,
        grid=(cols // tile,),
        in_specs=in_specs,
        out_specs=pl.BlockSpec((rows, tile), lambda j: (0, j)),
        out_shape=jax.ShapeDtypeStruct((rows, cols), jnp.float32),
        cost_estimate=pl.CostEstimate(
            flops=2 * rows * depth * cols,
            bytes_accessed=g.size * 2 + w.size * 2 + rows * cols * 4 * (2 if acc is not None else 1),
            transcendentals=0,
        ),
    )(*args)


def per_device(n_tok, acts, grad_out, weight, block_rows, block_cols, block_count):
    me = lax.axis_index("tok")
    tok_dev = acts.shape[0]
    sub = BLK // n_tok

    full_acts = lax.all_gather(acts, "feat", axis=1, tiled=True)
    row_blocks = full_acts.shape[1] // BLK
    acts_pieces = jnp.transpose(full_acts.reshape(tok_dev, row_blocks, n_tok, sub), (2, 1, 3, 0))

    f_chunk = grad_out.shape[1] // F_CHUNKS
    gathered = []
    partial_sums = None
    for k in range(F_CHUNKS):
        cols = slice(k * f_chunk, (k + 1) * f_chunk)
        piece = grad_out[:, cols]
        if gathered:
            piece, gathered[-1] = lax.optimization_barrier((piece, gathered[-1]))
        gathered.append(place_rows(xor_exchange(piece, "tok", n_tok), me))
    for k in range(F_CHUNKS):
        cols = slice(k * f_chunk, (k + 1) * f_chunk)
        partial_sums = matmul_nt(gathered[k], weight[:, cols], partial_sums)
    gout = jnp.concatenate(gathered, axis=1)
    grad_in = lax.psum_scatter(partial_sums, "feat", scatter_dimension=0, tiled=True).astype(
        jnp.bfloat16
    )

    acts_pieces, gout = lax.optimization_barrier((acts_pieces, gout))
    got = []
    for m in range(n_tok):
        part = lax.dynamic_index_in_dim(acts_pieces, me ^ m, axis=0, keepdims=False)
        if m:
            part = lax.ppermute(part, "tok", perm=[(a, a ^ m) for a in range(n_tok)])
        got.append(part)
    acts_t = place_rows(got, me, axis=2)
    block_grads = block_tiles(block_rows, block_cols, block_count, acts_t, gout)
    return (grad_in, block_grads)


def solution(mesh):
    n_tok = mesh.shape["tok"]
    assert n_tok & (n_tok - 1) == 0
    in_specs = (
        P("tok", "feat"),
        P("tok", "feat"),
        P("tok", "feat"),
        P("feat"),
        P("feat"),
        P("feat"),
    )
    out_specs = (P("feat", "tok"), P("feat", "tok", None))
    return jax.shard_map(
        functools.partial(per_device, n_tok),
        mesh=mesh,
        in_specs=in_specs,
        out_specs=out_specs,
        check_vma=False,
    )
```

```python
import functools

import jax
import jax.numpy as jnp
from jax import lax
from jax.experimental import pallas as pl
from jax.experimental.pallas import tpu as pltpu
from jax.sharding import PartitionSpec as P

BLK = 128
SLOTS_PER_STEP = 8
F_CHUNKS = 2


def xor_exchange(x, axis_name, n):
    out = [x]
    for m in range(1, n):
        out.append(lax.ppermute(x, axis_name, perm=[(a, a ^ m) for a in range(n)]))
    return out


def place_rows(pieces, me, axis=0):
    rows = pieces[0].shape[axis]
    shape = list(pieces[0].shape)
    shape[axis] = rows * len(pieces)
    out = jnp.zeros(shape, pieces[0].dtype)
    for m, piece in enumerate(pieces):
        out = lax.dynamic_update_slice_in_dim(out, piece, (me ^ m) * rows, axis)
    return out


def block_kernel(rows_ref, cols_ref, cnt_ref, a_ref, g_ref, o_ref):
    step = pl.program_id(0)
    for u in range(SLOTS_PER_STEP):
        s = step * SLOTS_PER_STEP + u
        a = a_ref[rows_ref[s]]
        g = g_ref[:, pl.ds(pl.multiple_of(cols_ref[s] * BLK, BLK), BLK)]
        tile = jnp.dot(a, g, preferred_element_type=jnp.float32)
        tile = jnp.where(s < cnt_ref[0], tile, jnp.float32(0.0))
        o_ref[u] = tile.astype(o_ref.dtype)


def block_tiles(rows, cols, count, acts_t, gout):
    n_slots = rows.shape[0]
    sub, tokens = acts_t.shape[1], acts_t.shape[2]
    grid_spec = pltpu.PrefetchScalarGridSpec(
        num_scalar_prefetch=3,
        grid=(n_slots // SLOTS_PER_STEP,),
        in_specs=[
            pl.BlockSpec(acts_t.shape, lambda g, r, c, n: (0, 0, 0)),
            pl.BlockSpec(gout.shape, lambda g, r, c, n: (0, 0)),
        ],
        out_specs=pl.BlockSpec((SLOTS_PER_STEP, sub, BLK), lambda g, r, c, n: (g, 0, 0)),
    )
    return pl.pallas_call(
        block_kernel,
        grid_spec=grid_spec,
        out_shape=jax.ShapeDtypeStruct((n_slots, sub, BLK), jnp.bfloat16),
        cost_estimate=pl.CostEstimate(
            flops=2 * n_slots * sub * tokens * BLK,
            bytes_accessed=acts_t.size * 2 + gout.size * 2 + n_slots * sub * BLK * 2,
            transcendentals=0,
        ),
    )(rows, cols, count, acts_t, gout)


def matmul_kernel(*refs):
    if len(refs) == 4:
        w_ref, g_ref, acc_ref, o_ref = refs
    else:
        (w_ref, g_ref, o_ref), acc_ref = refs, None
    out = jnp.dot(w_ref[...], g_ref[...], preferred_element_type=jnp.float32)
    if acc_ref is not None:
        out = out + acc_ref[...]
    o_ref[...] = out


def matmul_wg(w, g_t, k, acc):
    depth, tokens = g_t.shape
    rows = w.shape[0]
    tile = min(rows, 512)
    in_specs = [
        pl.BlockSpec((tile, depth), lambda j: (j, k)),
        pl.BlockSpec((depth, tokens), lambda j: (0, 0)),
    ]
    args = [w, g_t]
    if acc is not None:
        in_specs.append(pl.BlockSpec((tile, tokens), lambda j: (j, 0)))
        args.append(acc)
    return pl.pallas_call(
        matmul_kernel,
        grid=(rows // tile,),
        in_specs=in_specs,
        out_specs=pl.BlockSpec((tile, tokens), lambda j: (j, 0)),
        out_shape=jax.ShapeDtypeStruct((rows, tokens), jnp.float32),
        cost_estimate=pl.CostEstimate(
            flops=2 * rows * depth * tokens,
            bytes_accessed=rows * depth * 2
            + g_t.size * 2
            + rows * tokens * 4 * (2 if acc is not None else 1),
            transcendentals=0,
        ),
    )(*args)


def per_device(n_tok, acts, grad_out, weight, block_rows, block_cols, block_count):
    me = lax.axis_index("tok")
    tok_dev = acts.shape[0]
    sub = BLK // n_tok

    full_acts = lax.all_gather(acts, "feat", axis=1, tiled=True)
    row_blocks = full_acts.shape[1] // BLK
    acts_pieces = jnp.transpose(full_acts.reshape(tok_dev, row_blocks, n_tok, sub), (2, 1, 3, 0))

    f_chunk = grad_out.shape[1] // F_CHUNKS
    gathered = []
    for k in range(F_CHUNKS):
        piece = grad_out[:, k * f_chunk : (k + 1) * f_chunk]
        if gathered:
            piece, gathered[-1] = lax.optimization_barrier((piece, gathered[-1]))
        gathered.append(place_rows(xor_exchange(piece, "tok", n_tok), me))
    partial_t = None
    for k in range(F_CHUNKS):
        partial_t = matmul_wg(weight, gathered[k].T, k, partial_t)
    gout = jnp.concatenate(gathered, axis=1)
    grad_in = lax.psum_scatter(partial_t, "feat", scatter_dimension=1, tiled=True).T.astype(
        jnp.bfloat16
    )

    acts_pieces, gout = lax.optimization_barrier((acts_pieces, gout))
    got = []
    for m in range(n_tok):
        part = lax.dynamic_index_in_dim(acts_pieces, me ^ m, axis=0, keepdims=False)
        if m:
            part = lax.ppermute(part, "tok", perm=[(a, a ^ m) for a in range(n_tok)])
        got.append(part)
    acts_t = place_rows(got, me, axis=2)
    block_grads = block_tiles(block_rows, block_cols, block_count, acts_t, gout)
    return (grad_in, block_grads)


def solution(mesh):
    n_tok = mesh.shape["tok"]
    assert n_tok & (n_tok - 1) == 0
    in_specs = (
        P("tok", "feat"),
        P("tok", "feat"),
        P("tok", "feat"),
        P("feat"),
        P("feat"),
        P("feat"),
    )
    out_specs = (P("feat", "tok"), P("feat", "tok", None))
    return jax.shard_map(
        functools.partial(per_device, n_tok),
        mesh=mesh,
        in_specs=in_specs,
        out_specs=out_specs,
        check_vma=False,
    )
```

```python
import functools

import jax
import jax.numpy as jnp
from jax import lax
from jax.experimental import pallas as pl
from jax.experimental.pallas import tpu as pltpu
from jax.sharding import PartitionSpec as P

BLK = 128
SLOTS_PER_STEP = 8
F_CHUNKS = 2


def xor_exchange(x, axis_name, n):
    out = [x]
    for m in range(1, n):
        out.append(lax.ppermute(x, axis_name, perm=[(a, a ^ m) for a in range(n)]))
    return out


def place_rows(pieces, me, axis=0):
    rows = pieces[0].shape[axis]
    shape = list(pieces[0].shape)
    shape[axis] = rows * len(pieces)
    out = jnp.zeros(shape, pieces[0].dtype)
    for m, piece in enumerate(pieces):
        out = lax.dynamic_update_slice_in_dim(out, piece, (me ^ m) * rows, axis)
    return out


def block_kernel(rows_ref, cols_ref, cnt_ref, a_ref, g_ref, o_ref):
    step = pl.program_id(0)
    for u in range(SLOTS_PER_STEP):
        s = step * SLOTS_PER_STEP + u
        a = a_ref[rows_ref[s]]
        g = g_ref[:, pl.ds(pl.multiple_of(cols_ref[s] * BLK, BLK), BLK)]
        tile = jnp.dot(a, g, preferred_element_type=jnp.float32)
        tile = jnp.where(s < cnt_ref[0], tile, jnp.float32(0.0))
        o_ref[u] = tile.astype(o_ref.dtype)


def block_tiles(rows, cols, count, acts_t, gout):
    n_slots = rows.shape[0]
    sub, tokens = acts_t.shape[1], acts_t.shape[2]
    grid_spec = pltpu.PrefetchScalarGridSpec(
        num_scalar_prefetch=3,
        grid=(n_slots // SLOTS_PER_STEP,),
        in_specs=[
            pl.BlockSpec(acts_t.shape, lambda g, r, c, n: (0, 0, 0)),
            pl.BlockSpec(gout.shape, lambda g, r, c, n: (0, 0)),
        ],
        out_specs=pl.BlockSpec((SLOTS_PER_STEP, sub, BLK), lambda g, r, c, n: (g, 0, 0)),
    )
    return pl.pallas_call(
        block_kernel,
        grid_spec=grid_spec,
        out_shape=jax.ShapeDtypeStruct((n_slots, sub, BLK), jnp.bfloat16),
        cost_estimate=pl.CostEstimate(
            flops=2 * n_slots * sub * tokens * BLK,
            bytes_accessed=acts_t.size * 2 + gout.size * 2 + n_slots * sub * BLK * 2,
            transcendentals=0,
        ),
    )(rows, cols, count, acts_t, gout)


def matmul_kernel(*refs):
    if len(refs) == 4:
        g_ref, w_ref, acc_ref, o_ref = refs
    else:
        (g_ref, w_ref, o_ref), acc_ref = refs, None
    out = lax.dot_general(
        g_ref[...], w_ref[...], (((1,), (1,)), ((), ())), preferred_element_type=jnp.float32
    )
    if acc_ref is not None:
        out = out + acc_ref[...]
    o_ref[...] = out


def matmul_nt(g, w, k, acc):
    rows, depth = g.shape
    cols = w.shape[0]
    tile = min(cols, 512)
    in_specs = [
        pl.BlockSpec((rows, depth), lambda j: (0, 0)),
        pl.BlockSpec((tile, depth), lambda j: (j, k)),
    ]
    args = [g, w]
    if acc is not None:
        in_specs.append(pl.BlockSpec((rows, tile), lambda j: (0, j)))
        args.append(acc)
    return pl.pallas_call(
        matmul_kernel,
        grid=(cols // tile,),
        in_specs=in_specs,
        out_specs=pl.BlockSpec((rows, tile), lambda j: (0, j)),
        out_shape=jax.ShapeDtypeStruct((rows, cols), jnp.float32),
        cost_estimate=pl.CostEstimate(
            flops=2 * rows * depth * cols,
            bytes_accessed=g.size * 2 + cols * depth * 2 + rows * cols * 4 * (2 if acc is not None else 1),
            transcendentals=0,
        ),
    )(*args)


def per_device(n_tok, acts, grad_out, weight, block_rows, block_cols, block_count):
    me = lax.axis_index("tok")
    tok_dev = acts.shape[0]
    sub = BLK // n_tok

    full_acts = lax.all_gather(acts, "feat", axis=1, tiled=True)
    row_blocks = full_acts.shape[1] // BLK
    acts_pieces = jnp.transpose(full_acts.reshape(tok_dev, row_blocks, n_tok, sub), (2, 1, 3, 0))

    f_chunk = grad_out.shape[1] // F_CHUNKS
    gathered = []
    partial_sums = None
    for k in range(F_CHUNKS):
        cols = slice(k * f_chunk, (k + 1) * f_chunk)
        piece = grad_out[:, cols]
        if gathered:
            piece, gathered[-1] = lax.optimization_barrier((piece, gathered[-1]))
        gathered.append(place_rows(xor_exchange(piece, "tok", n_tok), me))
    for k in range(F_CHUNKS - 1):
        partial_sums = matmul_nt(gathered[k], weight, k, partial_sums)
    last = slice((F_CHUNKS - 1) * f_chunk, F_CHUNKS * f_chunk)
    partial_sums = partial_sums + lax.dot_general(
        gathered[-1], weight[:, last], (((1,), (1,)), ((), ())), preferred_element_type=jnp.float32
    )
    gout = jnp.concatenate(gathered, axis=1)
    grad_in = lax.psum_scatter(partial_sums, "feat", scatter_dimension=0, tiled=True).astype(
        jnp.bfloat16
    )

    acts_pieces, gout = lax.optimization_barrier((acts_pieces, gout))
    got = []
    for m in range(n_tok):
        part = lax.dynamic_index_in_dim(acts_pieces, me ^ m, axis=0, keepdims=False)
        if m:
            part = lax.ppermute(part, "tok", perm=[(a, a ^ m) for a in range(n_tok)])
        got.append(part)
    acts_t = place_rows(got, me, axis=2)
    block_grads = block_tiles(block_rows, block_cols, block_count, acts_t, gout)
    return (grad_in, block_grads)


def solution(mesh):
    n_tok = mesh.shape["tok"]
    assert n_tok & (n_tok - 1) == 0
    in_specs = (
        P("tok", "feat"),
        P("tok", "feat"),
        P("tok", "feat"),
        P("feat"),
        P("feat"),
        P("feat"),
    )
    out_specs = (P("feat", "tok"), P("feat", "tok", None))
    return jax.shard_map(
        functools.partial(per_device, n_tok),
        mesh=mesh,
        in_specs=in_specs,
        out_specs=out_specs,
        check_vma=False,
    )
```

```python
import functools

import jax
import jax.numpy as jnp
from jax import lax
from jax.experimental import pallas as pl
from jax.experimental.pallas import tpu as pltpu
from jax.sharding import PartitionSpec as P

BLK = 128
SLOTS_PER_STEP = 8


def xor_exchange(x, axis_name, n):
    out = [x]
    for m in range(1, n):
        out.append(lax.ppermute(x, axis_name, perm=[(a, a ^ m) for a in range(n)]))
    return out


def place_rows(pieces, me, axis=0):
    rows = pieces[0].shape[axis]
    shape = list(pieces[0].shape)
    shape[axis] = rows * len(pieces)
    out = jnp.zeros(shape, pieces[0].dtype)
    for m, piece in enumerate(pieces):
        out = lax.dynamic_update_slice_in_dim(out, piece, (me ^ m) * rows, axis)
    return out


def block_kernel(rows_ref, cols_ref, cnt_ref, a_ref, g_ref, o_ref):
    step = pl.program_id(0)
    for u in range(SLOTS_PER_STEP):
        s = step * SLOTS_PER_STEP + u
        a = a_ref[rows_ref[s]]
        g = g_ref[:, pl.ds(pl.multiple_of(cols_ref[s] * BLK, BLK), BLK)]
        tile = jnp.dot(a, g, preferred_element_type=jnp.float32)
        tile = jnp.where(s < cnt_ref[0], tile, jnp.float32(0.0))
        o_ref[u] = tile.astype(o_ref.dtype)


def block_tiles(rows, cols, count, acts_t, gout):
    n_slots = rows.shape[0]
    sub, tokens = acts_t.shape[1], acts_t.shape[2]
    grid_spec = pltpu.PrefetchScalarGridSpec(
        num_scalar_prefetch=3,
        grid=(n_slots // SLOTS_PER_STEP,),
        in_specs=[
            pl.BlockSpec(acts_t.shape, lambda g, r, c, n: (0, 0, 0)),
            pl.BlockSpec(gout.shape, lambda g, r, c, n: (0, 0)),
        ],
        out_specs=pl.BlockSpec((SLOTS_PER_STEP, sub, BLK), lambda g, r, c, n: (g, 0, 0)),
    )
    return pl.pallas_call(
        block_kernel,
        grid_spec=grid_spec,
        out_shape=jax.ShapeDtypeStruct((n_slots, sub, BLK), jnp.bfloat16),
        cost_estimate=pl.CostEstimate(
            flops=2 * n_slots * sub * tokens * BLK,
            bytes_accessed=acts_t.size * 2 + gout.size * 2 + n_slots * sub * BLK * 2,
            transcendentals=0,
        ),
    )(rows, cols, count, acts_t, gout)


def feat_all_gather(x, n_feat, me_feat):
    core = me_feat % 2
    zs = [x] + [
        lax.ppermute(x, "feat", perm=[(a, a ^ m) for a in range(n_feat)])
        for m in range(2, n_feat, 2)
    ]
    mine = place_rows([piece[None] for piece in zs], me_feat // 2, axis=0)
    other = lax.ppermute(mine, "feat", perm=[(a, a ^ 1) for a in range(n_feat)])
    both = place_rows([mine[:, None], other[:, None]], core, axis=1)
    return jnp.transpose(both, (2, 0, 1, 3)).reshape(x.shape[0], -1)


def chip_sum(h, n_feat, me_feat):
    core = me_feat % 2
    h = h.reshape((n_feat // 2, 2, h.shape[0] // n_feat) + h.shape[1:])
    send = lax.dynamic_index_in_dim(h, 1 - core, axis=1, keepdims=False)
    keep = lax.dynamic_index_in_dim(h, core, axis=1, keepdims=False)
    return keep + lax.ppermute(send, "feat", perm=[(a, a ^ 1) for a in range(n_feat)])


def z_reduce(chip, n_feat, me_feat):
    z = me_feat // 2
    total = lax.dynamic_index_in_dim(chip, z, axis=0, keepdims=False)
    for m in range(1, n_feat // 2):
        part = lax.dynamic_index_in_dim(chip, z ^ m, axis=0, keepdims=False)
        total = total + lax.ppermute(part, "feat", perm=[(a, a ^ (2 * m)) for a in range(n_feat)])
    return total


def per_device(n_tok, n_feat, acts, grad_out, weight, block_rows, block_cols, block_count):
    me = lax.axis_index("tok")
    me_feat = lax.axis_index("feat")
    tok_dev = acts.shape[0]
    sub = BLK // n_tok

    full_acts = feat_all_gather(acts, n_feat, me_feat)
    row_blocks = full_acts.shape[1] // BLK
    acts_pieces = jnp.transpose(full_acts.reshape(tok_dev, row_blocks, n_tok, sub), (2, 1, 3, 0))

    gout = place_rows(xor_exchange(grad_out, "tok", n_tok), me)

    acts_pieces, gout = lax.optimization_barrier((acts_pieces, gout))
    got = []
    for m in range(n_tok):
        part = lax.dynamic_index_in_dim(acts_pieces, me ^ m, axis=0, keepdims=False)
        if m:
            part = lax.ppermute(part, "tok", perm=[(a, a ^ m) for a in range(n_tok)])
        got.append(part)
    acts_t = place_rows(got, me, axis=2)

    chips = []
    d_half = weight.shape[0] // 2
    for k in range(2):
        partial_sums = lax.dot_general(
            gout,
            weight[k * d_half : (k + 1) * d_half],
            (((1,), (1,)), ((), ())),
            preferred_element_type=jnp.float32,
        )
        chips.append(chip_sum(partial_sums, n_feat, me_feat))
    halves = [z_reduce(chip, n_feat, me_feat) for chip in chips]
    grad_in = jnp.concatenate(halves, axis=1).astype(jnp.bfloat16)

    acts_t, gout_b, _ = lax.optimization_barrier((acts_t, gout, chips[1]))
    block_grads = block_tiles(block_rows, block_cols, block_count, acts_t, gout_b)
    return (grad_in, block_grads)


def solution(mesh):
    n_tok = mesh.shape["tok"]
    n_feat = mesh.shape["feat"]
    assert n_tok & (n_tok - 1) == 0 and n_feat & (n_feat - 1) == 0
    in_specs = (
        P("tok", "feat"),
        P("tok", "feat"),
        P("tok", "feat"),
        P("feat"),
        P("feat"),
        P("feat"),
    )
    out_specs = (P("feat", "tok"), P("feat", "tok", None))
    return jax.shard_map(
        functools.partial(per_device, n_tok, n_feat),
        mesh=mesh,
        in_specs=in_specs,
        out_specs=out_specs,
        check_vma=False,
    )
```

```python
import functools

import jax
import jax.numpy as jnp
from jax import lax
from jax.experimental import pallas as pl
from jax.experimental.pallas import tpu as pltpu
from jax.sharding import PartitionSpec as P

BLK = 128
SLOTS_PER_STEP = 8


def xor_exchange(x, axis_name, n):
    out = [x]
    for m in range(1, n):
        out.append(lax.ppermute(x, axis_name, perm=[(a, a ^ m) for a in range(n)]))
    return out


def place_rows(pieces, me, axis=0):
    rows = pieces[0].shape[axis]
    shape = list(pieces[0].shape)
    shape[axis] = rows * len(pieces)
    out = jnp.zeros(shape, pieces[0].dtype)
    for m, piece in enumerate(pieces):
        out = lax.dynamic_update_slice_in_dim(out, piece, (me ^ m) * rows, axis)
    return out


def block_kernel(rows_ref, cols_ref, cnt_ref, a_ref, g_ref, o_ref):
    step = pl.program_id(0)
    for u in range(SLOTS_PER_STEP):
        s = step * SLOTS_PER_STEP + u
        a = a_ref[rows_ref[s]]
        g = g_ref[:, pl.ds(pl.multiple_of(cols_ref[s] * BLK, BLK), BLK)]
        tile = jnp.dot(a, g, preferred_element_type=jnp.float32)
        tile = jnp.where(s < cnt_ref[0], tile, jnp.float32(0.0))
        o_ref[u] = tile.astype(o_ref.dtype)


def block_tiles(rows, cols, count, acts_t, gout):
    n_slots = rows.shape[0]
    sub, tokens = acts_t.shape[1], acts_t.shape[2]
    grid_spec = pltpu.PrefetchScalarGridSpec(
        num_scalar_prefetch=3,
        grid=(n_slots // SLOTS_PER_STEP,),
        in_specs=[
            pl.BlockSpec(acts_t.shape, lambda g, r, c, n: (0, 0, 0)),
            pl.BlockSpec(gout.shape, lambda g, r, c, n: (0, 0)),
        ],
        out_specs=pl.BlockSpec((SLOTS_PER_STEP, sub, BLK), lambda g, r, c, n: (g, 0, 0)),
    )
    return pl.pallas_call(
        block_kernel,
        grid_spec=grid_spec,
        out_shape=jax.ShapeDtypeStruct((n_slots, sub, BLK), jnp.bfloat16),
        cost_estimate=pl.CostEstimate(
            flops=2 * n_slots * sub * tokens * BLK,
            bytes_accessed=acts_t.size * 2 + gout.size * 2 + n_slots * sub * BLK * 2,
            transcendentals=0,
        ),
    )(rows, cols, count, acts_t, gout)


def matmul_kernel(*refs):
    if len(refs) == 4:
        g_ref, w_ref, acc_ref, o_ref = refs
    else:
        (g_ref, w_ref, o_ref), acc_ref = refs, None
    out = lax.dot_general(
        g_ref[...], w_ref[...], (((1,), (1,)), ((), ())), preferred_element_type=jnp.float32
    )
    if acc_ref is not None:
        out = out + acc_ref[...]
    o_ref[...] = out


def matmul_nt(g, w, k, acc):
    rows, depth = g.shape
    cols = w.shape[0]
    tile = min(cols, 512)
    in_specs = [
        pl.BlockSpec((rows, depth), lambda j: (0, 0)),
        pl.BlockSpec((tile, depth), lambda j: (j, k)),
    ]
    args = [g, w]
    if acc is not None:
        in_specs.append(pl.BlockSpec((rows, tile), lambda j: (0, j)))
        args.append(acc)
    return pl.pallas_call(
        matmul_kernel,
        grid=(cols // tile,),
        in_specs=in_specs,
        out_specs=pl.BlockSpec((rows, tile), lambda j: (0, j)),
        out_shape=jax.ShapeDtypeStruct((rows, cols), jnp.float32),
        cost_estimate=pl.CostEstimate(
            flops=2 * rows * depth * cols,
            bytes_accessed=g.size * 2 + cols * depth * 2 + rows * cols * 4 * (2 if acc is not None else 1),
            transcendentals=0,
        ),
    )(*args)


def per_device(n_tok, acts, grad_out, weight, block_rows, block_cols, block_count):
    me = lax.axis_index("tok")
    tok_dev = acts.shape[0]
    sub = BLK // n_tok

    full_acts = lax.all_gather(acts, "feat", axis=1, tiled=True)
    row_blocks = full_acts.shape[1] // BLK
    acts_pieces = jnp.transpose(full_acts.reshape(tok_dev, row_blocks, n_tok, sub), (2, 1, 3, 0))

    units = grad_out.shape[1] // BLK
    last = units // 7
    sizes = [(units - 3 * last) * BLK, 2 * last * BLK, last * BLK]
    gathered = []
    start = 0
    for size in sizes:
        piece = grad_out[:, start : start + size]
        if gathered:
            piece, gathered[-1] = lax.optimization_barrier((piece, gathered[-1]))
        gathered.append(place_rows(xor_exchange(piece, "tok", n_tok), me))
        start += size
    partial_sums = None
    start = 0
    for size, g in zip(sizes, gathered):
        partial_sums = matmul_nt(g, weight, start // size, partial_sums)
        start += size
    gout = jnp.concatenate(gathered, axis=1)
    grad_in = lax.psum_scatter(partial_sums, "feat", scatter_dimension=0, tiled=True).astype(
        jnp.bfloat16
    )

    acts_pieces, gout = lax.optimization_barrier((acts_pieces, gout))
    got = []
    for m in range(n_tok):
        part = lax.dynamic_index_in_dim(acts_pieces, me ^ m, axis=0, keepdims=False)
        if m:
            part = lax.ppermute(part, "tok", perm=[(a, a ^ m) for a in range(n_tok)])
        got.append(part)
    acts_t = place_rows(got, me, axis=2)
    block_grads = block_tiles(block_rows, block_cols, block_count, acts_t, gout)
    return (grad_in, block_grads)


def solution(mesh):
    n_tok = mesh.shape["tok"]
    assert n_tok & (n_tok - 1) == 0
    in_specs = (
        P("tok", "feat"),
        P("tok", "feat"),
        P("tok", "feat"),
        P("feat"),
        P("feat"),
        P("feat"),
    )
    out_specs = (P("feat", "tok"), P("feat", "tok", None))
    return jax.shard_map(
        functools.partial(per_device, n_tok),
        mesh=mesh,
        in_specs=in_specs,
        out_specs=out_specs,
        check_vma=False,
    )
```

```python
import functools

import jax
import jax.numpy as jnp
from jax import lax
from jax.experimental import pallas as pl
from jax.experimental.pallas import tpu as pltpu
from jax.sharding import PartitionSpec as P

BLK = 128
SLOTS_PER_STEP = 8


def xor_exchange(x, axis_name, n):
    out = [x]
    for m in range(1, n):
        out.append(lax.ppermute(x, axis_name, perm=[(a, a ^ m) for a in range(n)]))
    return out


def place_rows(pieces, me, axis=0):
    rows = pieces[0].shape[axis]
    shape = list(pieces[0].shape)
    shape[axis] = rows * len(pieces)
    out = jnp.zeros(shape, pieces[0].dtype)
    for m, piece in enumerate(pieces):
        out = lax.dynamic_update_slice_in_dim(out, piece, (me ^ m) * rows, axis)
    return out


def block_kernel(rows_ref, cols_ref, cnt_ref, a_ref, g_ref, o_ref):
    step = pl.program_id(0)
    for u in range(SLOTS_PER_STEP):
        s = step * SLOTS_PER_STEP + u
        a = a_ref[rows_ref[s]]
        g = g_ref[:, pl.ds(pl.multiple_of(cols_ref[s] * BLK, BLK), BLK)]
        tile = jnp.dot(a, g, preferred_element_type=jnp.float32)
        tile = jnp.where(s < cnt_ref[0], tile, jnp.float32(0.0))
        o_ref[u] = tile.astype(o_ref.dtype)


def block_tiles(rows, cols, count, acts_t, gout):
    n_slots = rows.shape[0]
    sub, tokens = acts_t.shape[1], acts_t.shape[2]
    grid_spec = pltpu.PrefetchScalarGridSpec(
        num_scalar_prefetch=3,
        grid=(n_slots // SLOTS_PER_STEP,),
        in_specs=[
            pl.BlockSpec(acts_t.shape, lambda g, r, c, n: (0, 0, 0)),
            pl.BlockSpec(gout.shape, lambda g, r, c, n: (0, 0)),
        ],
        out_specs=pl.BlockSpec((SLOTS_PER_STEP, sub, BLK), lambda g, r, c, n: (g, 0, 0)),
    )
    return pl.pallas_call(
        block_kernel,
        grid_spec=grid_spec,
        out_shape=jax.ShapeDtypeStruct((n_slots, sub, BLK), jnp.bfloat16),
        cost_estimate=pl.CostEstimate(
            flops=2 * n_slots * sub * tokens * BLK,
            bytes_accessed=acts_t.size * 2 + gout.size * 2 + n_slots * sub * BLK * 2,
            transcendentals=0,
        ),
    )(rows, cols, count, acts_t, gout)


def per_device(n_tok, acts, grad_out, weight, block_rows, block_cols, block_count):
    me = lax.axis_index("tok")
    tok_dev = acts.shape[0]
    sub = BLK // n_tok

    full_acts = lax.all_gather(acts, "feat", axis=1, tiled=True)
    row_blocks = full_acts.shape[1] // BLK
    acts_pieces = jnp.transpose(full_acts.reshape(tok_dev, row_blocks, n_tok, sub), (2, 1, 3, 0))

    pieces = xor_exchange(grad_out, "tok", n_tok)
    gout = place_rows(pieces, me)

    def nt(x):
        return lax.dot_general(x, weight, (((1,), (1,)), ((), ())), preferred_element_type=jnp.float32)

    own = nt(grad_out)
    rest = nt(jnp.concatenate(pieces[1:], axis=0)).reshape(n_tok - 1, tok_dev, -1)
    partial_sums = place_rows([own] + [rest[m] for m in range(n_tok - 1)], me)
    grad_in = lax.psum_scatter(partial_sums, "feat", scatter_dimension=0, tiled=True).astype(
        jnp.bfloat16
    )

    acts_pieces, gout = lax.optimization_barrier((acts_pieces, gout))
    got = []
    for m in range(n_tok):
        part = lax.dynamic_index_in_dim(acts_pieces, me ^ m, axis=0, keepdims=False)
        if m:
            part = lax.ppermute(part, "tok", perm=[(a, a ^ m) for a in range(n_tok)])
        got.append(part)
    acts_t = place_rows(got, me, axis=2)
    block_grads = block_tiles(block_rows, block_cols, block_count, acts_t, gout)
    return (grad_in, block_grads)


def solution(mesh):
    n_tok = mesh.shape["tok"]
    assert n_tok & (n_tok - 1) == 0
    in_specs = (
        P("tok", "feat"),
        P("tok", "feat"),
        P("tok", "feat"),
        P("feat"),
        P("feat"),
        P("feat"),
    )
    out_specs = (P("feat", "tok"), P("feat", "tok", None))
    return jax.shard_map(
        functools.partial(per_device, n_tok),
        mesh=mesh,
        in_specs=in_specs,
        out_specs=out_specs,
        check_vma=False,
    )
```

```python
import functools

import jax
import jax.numpy as jnp
from jax import lax
from jax.experimental import pallas as pl
from jax.experimental.pallas import tpu as pltpu
from jax.sharding import PartitionSpec as P

BLK = 128
SLOTS_PER_STEP = 8


def xor_exchange(x, axis_name, n):
    out = [x]
    for m in range(1, n):
        out.append(lax.ppermute(x, axis_name, perm=[(a, a ^ m) for a in range(n)]))
    return out


def place_rows(pieces, me, axis=0):
    rows = pieces[0].shape[axis]
    shape = list(pieces[0].shape)
    shape[axis] = rows * len(pieces)
    out = jnp.zeros(shape, pieces[0].dtype)
    for m, piece in enumerate(pieces):
        out = lax.dynamic_update_slice_in_dim(out, piece, (me ^ m) * rows, axis)
    return out


def block_kernel(rows_ref, cols_ref, cnt_ref, a_ref, g_ref, o_ref):
    step = pl.program_id(0)
    for u in range(SLOTS_PER_STEP):
        s = step * SLOTS_PER_STEP + u
        a = a_ref[rows_ref[s]]
        g = g_ref[:, pl.ds(pl.multiple_of(cols_ref[s] * BLK, BLK), BLK)]
        tile = jnp.dot(a, g, preferred_element_type=jnp.float32)
        tile = jnp.where(s < cnt_ref[0], tile, jnp.float32(0.0))
        o_ref[u] = tile.astype(o_ref.dtype)


def block_tiles(rows, cols, count, acts_t, gout):
    n_slots = rows.shape[0]
    sub, tokens = acts_t.shape[1], acts_t.shape[2]
    grid_spec = pltpu.PrefetchScalarGridSpec(
        num_scalar_prefetch=3,
        grid=(n_slots // SLOTS_PER_STEP,),
        in_specs=[
            pl.BlockSpec(acts_t.shape, lambda g, r, c, n: (0, 0, 0)),
            pl.BlockSpec(gout.shape, lambda g, r, c, n: (0, 0)),
        ],
        out_specs=pl.BlockSpec((SLOTS_PER_STEP, sub, BLK), lambda g, r, c, n: (g, 0, 0)),
    )
    return pl.pallas_call(
        block_kernel,
        grid_spec=grid_spec,
        out_shape=jax.ShapeDtypeStruct((n_slots, sub, BLK), jnp.bfloat16),
        cost_estimate=pl.CostEstimate(
            flops=2 * n_slots * sub * tokens * BLK,
            bytes_accessed=acts_t.size * 2 + gout.size * 2 + n_slots * sub * BLK * 2,
            transcendentals=0,
        ),
    )(rows, cols, count, acts_t, gout)


def per_device(n_tok, acts, grad_out, weight, block_rows, block_cols, block_count):
    me = lax.axis_index("tok")
    tok_dev = acts.shape[0]
    sub = BLK // n_tok

    full_acts = lax.all_gather(acts, "feat", axis=1, tiled=True)
    row_blocks = full_acts.shape[1] // BLK
    acts_pieces = jnp.transpose(full_acts.reshape(tok_dev, row_blocks, n_tok, sub), (2, 1, 3, 0))

    pieces = xor_exchange(grad_out, "tok", n_tok)
    gout = place_rows(pieces, me)

    def nt(x):
        return lax.dot_general(x, weight, (((1,), (1,)), ((), ())), preferred_element_type=jnp.float32)

    own = nt(grad_out)
    first = nt(pieces[1])
    rest = nt(jnp.concatenate(pieces[2:], axis=0)).reshape(n_tok - 2, tok_dev, -1)
    partial_sums = place_rows([own, first] + [rest[m] for m in range(n_tok - 2)], me)
    grad_in = lax.psum_scatter(partial_sums, "feat", scatter_dimension=0, tiled=True).astype(
        jnp.bfloat16
    )

    acts_pieces, gout = lax.optimization_barrier((acts_pieces, gout))
    got = []
    for m in range(n_tok):
        part = lax.dynamic_index_in_dim(acts_pieces, me ^ m, axis=0, keepdims=False)
        if m:
            part = lax.ppermute(part, "tok", perm=[(a, a ^ m) for a in range(n_tok)])
        got.append(part)
    acts_t = place_rows(got, me, axis=2)
    block_grads = block_tiles(block_rows, block_cols, block_count, acts_t, gout)
    return (grad_in, block_grads)


def solution(mesh):
    n_tok = mesh.shape["tok"]
    assert n_tok & (n_tok - 1) == 0
    in_specs = (
        P("tok", "feat"),
        P("tok", "feat"),
        P("tok", "feat"),
        P("feat"),
        P("feat"),
        P("feat"),
    )
    out_specs = (P("feat", "tok"), P("feat", "tok", None))
    return jax.shard_map(
        functools.partial(per_device, n_tok),
        mesh=mesh,
        in_specs=in_specs,
        out_specs=out_specs,
        check_vma=False,
    )
```

```python
import functools

import jax
import jax.numpy as jnp
from jax import lax
from jax.experimental import pallas as pl
from jax.experimental.pallas import tpu as pltpu
from jax.sharding import PartitionSpec as P

BLK = 128
SLOTS_PER_STEP = 8


def xor_exchange(x, axis_name, n):
    out = [x]
    for m in range(1, n):
        out.append(lax.ppermute(x, axis_name, perm=[(a, a ^ m) for a in range(n)]))
    return out


def place_rows(pieces, me, axis=0):
    rows = pieces[0].shape[axis]
    shape = list(pieces[0].shape)
    shape[axis] = rows * len(pieces)
    out = jnp.zeros(shape, pieces[0].dtype)
    for m, piece in enumerate(pieces):
        out = lax.dynamic_update_slice_in_dim(out, piece, (me ^ m) * rows, axis)
    return out


def block_kernel(rows_ref, cols_ref, cnt_ref, a_ref, g_ref, o_ref):
    step = pl.program_id(0)
    for u in range(SLOTS_PER_STEP):
        s = step * SLOTS_PER_STEP + u
        a = a_ref[rows_ref[s]]
        g = g_ref[:, pl.ds(pl.multiple_of(cols_ref[s] * BLK, BLK), BLK)]
        tile = jnp.dot(a, g, preferred_element_type=jnp.float32)
        tile = jnp.where(s < cnt_ref[0], tile, jnp.float32(0.0))
        o_ref[u] = tile.astype(o_ref.dtype)


def block_tiles(rows, cols, count, acts_t, gout):
    n_slots = rows.shape[0]
    sub, tokens = acts_t.shape[1], acts_t.shape[2]
    grid_spec = pltpu.PrefetchScalarGridSpec(
        num_scalar_prefetch=3,
        grid=(n_slots // SLOTS_PER_STEP,),
        in_specs=[
            pl.BlockSpec(acts_t.shape, lambda g, r, c, n: (0, 0, 0)),
            pl.BlockSpec(gout.shape, lambda g, r, c, n: (0, 0)),
        ],
        out_specs=pl.BlockSpec((SLOTS_PER_STEP, sub, BLK), lambda g, r, c, n: (g, 0, 0)),
    )
    return pl.pallas_call(
        block_kernel,
        grid_spec=grid_spec,
        out_shape=jax.ShapeDtypeStruct((n_slots, sub, BLK), jnp.bfloat16),
        cost_estimate=pl.CostEstimate(
            flops=2 * n_slots * sub * tokens * BLK,
            bytes_accessed=acts_t.size * 2 + gout.size * 2 + n_slots * sub * BLK * 2,
            transcendentals=0,
        ),
    )(rows, cols, count, acts_t, gout)


def per_device(n_tok, acts, grad_out, weight, block_rows, block_cols, block_count):
    me = lax.axis_index("tok")
    tok_dev = acts.shape[0]
    sub = BLK // n_tok

    full_acts = lax.all_gather(acts, "feat", axis=1, tiled=True)
    row_blocks = full_acts.shape[1] // BLK
    acts_pieces = jnp.transpose(full_acts.reshape(tok_dev, row_blocks, n_tok, sub), (2, 1, 3, 0))

    pieces = xor_exchange(grad_out, "tok", n_tok)
    gout = place_rows(pieces, me)

    def nt(x):
        return lax.dot_general(x, weight, (((1,), (1,)), ((), ())), preferred_element_type=jnp.float32)

    half = n_tok // 2
    partial_sums = jnp.zeros((n_tok * tok_dev, weight.shape[0]), jnp.float32)
    for m in range(half):
        partial_sums = lax.dynamic_update_slice_in_dim(
            partial_sums, nt(pieces[m]), (me ^ m) * tok_dev, 0
        )
    far_pieces, partial_sums = lax.optimization_barrier((pieces[half:], partial_sums))
    far = nt(jnp.concatenate(far_pieces, axis=0))
    for bit in range(half.bit_length() - 1):
        step = 1 << bit
        swapped = far.reshape(half // (2 * step), 2, step * tok_dev, -1)[:, ::-1].reshape(far.shape)
        far = jnp.where((me >> bit) % 2 == 1, swapped, far)
    base = ((me ^ half) // half) * half
    partial_sums = lax.dynamic_update_slice_in_dim(partial_sums, far, base * tok_dev, 0)
    grad_in = lax.psum_scatter(partial_sums, "feat", scatter_dimension=0, tiled=True).astype(
        jnp.bfloat16
    )

    acts_pieces, gout = lax.optimization_barrier((acts_pieces, gout))
    got = []
    for m in range(n_tok):
        part = lax.dynamic_index_in_dim(acts_pieces, me ^ m, axis=0, keepdims=False)
        if m:
            part = lax.ppermute(part, "tok", perm=[(a, a ^ m) for a in range(n_tok)])
        got.append(part)
    acts_t = place_rows(got, me, axis=2)
    block_grads = block_tiles(block_rows, block_cols, block_count, acts_t, gout)
    return (grad_in, block_grads)


def solution(mesh):
    n_tok = mesh.shape["tok"]
    assert n_tok & (n_tok - 1) == 0
    in_specs = (
        P("tok", "feat"),
        P("tok", "feat"),
        P("tok", "feat"),
        P("feat"),
        P("feat"),
        P("feat"),
    )
    out_specs = (P("feat", "tok"), P("feat", "tok", None))
    return jax.shard_map(
        functools.partial(per_device, n_tok),
        mesh=mesh,
        in_specs=in_specs,
        out_specs=out_specs,
        check_vma=False,
    )
```

```python
import functools

import jax
import jax.numpy as jnp
from jax import lax
from jax.experimental import pallas as pl
from jax.experimental.pallas import tpu as pltpu
from jax.sharding import PartitionSpec as P

BLK = 128
SLOTS_PER_STEP = 8


def xor_exchange(x, axis_name, n):
    out = [x]
    for m in range(1, n):
        out.append(lax.ppermute(x, axis_name, perm=[(a, a ^ m) for a in range(n)]))
    return out


def place_rows(pieces, me, axis=0):
    rows = pieces[0].shape[axis]
    shape = list(pieces[0].shape)
    shape[axis] = rows * len(pieces)
    out = jnp.zeros(shape, pieces[0].dtype)
    for m, piece in enumerate(pieces):
        out = lax.dynamic_update_slice_in_dim(out, piece, (me ^ m) * rows, axis)
    return out


def block_kernel(rows_ref, cols_ref, cnt_ref, a_ref, g_ref, o_ref):
    step = pl.program_id(0)
    for u in range(SLOTS_PER_STEP):
        s = step * SLOTS_PER_STEP + u
        a = a_ref[rows_ref[s]]
        g = g_ref[:, pl.ds(pl.multiple_of(cols_ref[s] * BLK, BLK), BLK)]
        tile = jnp.dot(a, g, preferred_element_type=jnp.float32)
        tile = jnp.where(s < cnt_ref[0], tile, jnp.float32(0.0))
        o_ref[u] = tile.astype(o_ref.dtype)


def block_tiles(rows, cols, count, acts_t, gout):
    n_slots = rows.shape[0]
    sub, tokens = acts_t.shape[1], acts_t.shape[2]
    grid_spec = pltpu.PrefetchScalarGridSpec(
        num_scalar_prefetch=3,
        grid=(n_slots // SLOTS_PER_STEP,),
        in_specs=[
            pl.BlockSpec(acts_t.shape, lambda g, r, c, n: (0, 0, 0)),
            pl.BlockSpec(gout.shape, lambda g, r, c, n: (0, 0)),
        ],
        out_specs=pl.BlockSpec((SLOTS_PER_STEP, sub, BLK), lambda g, r, c, n: (g, 0, 0)),
    )
    return pl.pallas_call(
        block_kernel,
        grid_spec=grid_spec,
        out_shape=jax.ShapeDtypeStruct((n_slots, sub, BLK), jnp.bfloat16),
        cost_estimate=pl.CostEstimate(
            flops=2 * n_slots * sub * tokens * BLK,
            bytes_accessed=acts_t.size * 2 + gout.size * 2 + n_slots * sub * BLK * 2,
            transcendentals=0,
        ),
    )(rows, cols, count, acts_t, gout)


def per_device(n_tok, acts, grad_out, weight, block_rows, block_cols, block_count):
    me = lax.axis_index("tok")
    tok_dev = acts.shape[0]
    sub = BLK // n_tok

    full_acts = lax.all_gather(acts, "feat", axis=1, tiled=True)
    row_blocks = full_acts.shape[1] // BLK
    acts_pieces = jnp.transpose(full_acts.reshape(tok_dev, row_blocks, n_tok, sub), (2, 1, 3, 0))

    pieces = [grad_out] + [
        lax.ppermute(grad_out, "tok", perm=[(a, a ^ m) for a in range(n_tok)]) for m in range(1, n_tok - 1)
    ]
    late, pieces[n_tok // 2] = lax.optimization_barrier((grad_out, pieces[n_tok // 2]))
    pieces.append(lax.ppermute(late, "tok", perm=[(a, a ^ (n_tok - 1)) for a in range(n_tok)]))
    gout = place_rows(pieces, me)

    def nt(x):
        return lax.dot_general(x, weight, (((1,), (1,)), ((), ())), preferred_element_type=jnp.float32)

    own = nt(grad_out)
    first = nt(pieces[1])
    rest = nt(jnp.concatenate(pieces[2:], axis=0)).reshape(n_tok - 2, tok_dev, -1)
    partial_sums = place_rows([own, first] + [rest[m] for m in range(n_tok - 2)], me)
    grad_in = lax.psum_scatter(partial_sums, "feat", scatter_dimension=0, tiled=True).astype(
        jnp.bfloat16
    )

    acts_pieces, gout = lax.optimization_barrier((acts_pieces, gout))
    got = []
    for m in range(n_tok):
        part = lax.dynamic_index_in_dim(acts_pieces, me ^ m, axis=0, keepdims=False)
        if m:
            part = lax.ppermute(part, "tok", perm=[(a, a ^ m) for a in range(n_tok)])
        got.append(part)
    acts_t = place_rows(got, me, axis=2)
    block_grads = block_tiles(block_rows, block_cols, block_count, acts_t, gout)
    return (grad_in, block_grads)


def solution(mesh):
    n_tok = mesh.shape["tok"]
    assert n_tok & (n_tok - 1) == 0
    in_specs = (
        P("tok", "feat"),
        P("tok", "feat"),
        P("tok", "feat"),
        P("feat"),
        P("feat"),
        P("feat"),
    )
    out_specs = (P("feat", "tok"), P("feat", "tok", None))
    return jax.shard_map(
        functools.partial(per_device, n_tok),
        mesh=mesh,
        in_specs=in_specs,
        out_specs=out_specs,
        check_vma=False,
    )
```

```python
import functools

import jax
import jax.numpy as jnp
from jax import lax
from jax.experimental import pallas as pl
from jax.experimental.pallas import tpu as pltpu
from jax.sharding import PartitionSpec as P

BLK = 128
SLOTS_PER_STEP = 8


def xor_exchange(x, axis_name, n):
    out = [x]
    for m in range(1, n):
        out.append(lax.ppermute(x, axis_name, perm=[(a, a ^ m) for a in range(n)]))
    return out


def place_rows(pieces, me, axis=0):
    rows = pieces[0].shape[axis]
    shape = list(pieces[0].shape)
    shape[axis] = rows * len(pieces)
    out = jnp.zeros(shape, pieces[0].dtype)
    for m, piece in enumerate(pieces):
        out = lax.dynamic_update_slice_in_dim(out, piece, (me ^ m) * rows, axis)
    return out


def block_kernel(rows_ref, cols_ref, cnt_ref, a_ref, g_ref, o_ref):
    step = pl.program_id(0)
    for u in range(SLOTS_PER_STEP):
        s = step * SLOTS_PER_STEP + u
        a = a_ref[rows_ref[s]]
        g = g_ref[:, pl.ds(pl.multiple_of(cols_ref[s] * BLK, BLK), BLK)]
        tile = jnp.dot(a, g, preferred_element_type=jnp.float32)
        tile = jnp.where(s < cnt_ref[0], tile, jnp.float32(0.0))
        o_ref[u] = tile.astype(o_ref.dtype)


def block_tiles(rows, cols, count, acts_t, gout):
    n_slots = rows.shape[0]
    sub, tokens = acts_t.shape[1], acts_t.shape[2]
    grid_spec = pltpu.PrefetchScalarGridSpec(
        num_scalar_prefetch=3,
        grid=(n_slots // SLOTS_PER_STEP,),
        in_specs=[
            pl.BlockSpec(acts_t.shape, lambda g, r, c, n: (0, 0, 0)),
            pl.BlockSpec(gout.shape, lambda g, r, c, n: (0, 0)),
        ],
        out_specs=pl.BlockSpec((SLOTS_PER_STEP, sub, BLK), lambda g, r, c, n: (g, 0, 0)),
    )
    return pl.pallas_call(
        block_kernel,
        grid_spec=grid_spec,
        out_shape=jax.ShapeDtypeStruct((n_slots, sub, BLK), jnp.bfloat16),
        cost_estimate=pl.CostEstimate(
            flops=2 * n_slots * sub * tokens * BLK,
            bytes_accessed=acts_t.size * 2 + gout.size * 2 + n_slots * sub * BLK * 2,
            transcendentals=0,
        ),
    )(rows, cols, count, acts_t, gout)


def per_device(n_tok, acts, grad_out, weight, block_rows, block_cols, block_count):
    me = lax.axis_index("tok")
    tok_dev = acts.shape[0]
    sub = BLK // n_tok

    full_acts = lax.all_gather(acts, "feat", axis=1, tiled=True)
    row_blocks = full_acts.shape[1] // BLK
    acts_pieces = jnp.transpose(full_acts.reshape(tok_dev, row_blocks, n_tok, sub), (2, 1, 3, 0))

    pieces = xor_exchange(grad_out, "tok", n_tok)
    gout = place_rows(pieces, me)

    def nt(x):
        return lax.dot_general(x, weight, (((1,), (1,)), ((), ())), preferred_element_type=jnp.float32)

    half = n_tok // 2
    partial_sums = jnp.zeros((n_tok * tok_dev, weight.shape[0]), jnp.float32)
    for m in range(half):
        partial_sums = lax.dynamic_update_slice_in_dim(
            partial_sums, nt(pieces[m]), (me ^ m) * tok_dev, 0
        )
    far_pieces, partial_sums = lax.optimization_barrier((pieces[half:], partial_sums))
    far_in = jnp.zeros((half * tok_dev, grad_out.shape[1]), grad_out.dtype)
    for k, piece in enumerate(far_pieces):
        far_in = lax.dynamic_update_slice_in_dim(far_in, piece, ((me ^ (half + k)) % half) * tok_dev, 0)
    far = nt(far_in)
    base = ((me ^ half) // half) * half
    partial_sums = lax.dynamic_update_slice_in_dim(partial_sums, far, base * tok_dev, 0)
    grad_in = lax.psum_scatter(partial_sums, "feat", scatter_dimension=0, tiled=True).astype(
        jnp.bfloat16
    )

    acts_pieces, gout = lax.optimization_barrier((acts_pieces, gout))
    got = []
    for m in range(n_tok):
        part = lax.dynamic_index_in_dim(acts_pieces, me ^ m, axis=0, keepdims=False)
        if m:
            part = lax.ppermute(part, "tok", perm=[(a, a ^ m) for a in range(n_tok)])
        got.append(part)
    acts_t = place_rows(got, me, axis=2)
    block_grads = block_tiles(block_rows, block_cols, block_count, acts_t, gout)
    return (grad_in, block_grads)


def solution(mesh):
    n_tok = mesh.shape["tok"]
    assert n_tok & (n_tok - 1) == 0
    in_specs = (
        P("tok", "feat"),
        P("tok", "feat"),
        P("tok", "feat"),
        P("feat"),
        P("feat"),
        P("feat"),
    )
    out_specs = (P("feat", "tok"), P("feat", "tok", None))
    return jax.shard_map(
        functools.partial(per_device, n_tok),
        mesh=mesh,
        in_specs=in_specs,
        out_specs=out_specs,
        check_vma=False,
    )
```
